512 devices in a mesh: seq: 32 (over y, z_hi, core), chan: 16 (over x, z_lo).
Axes of the slice: x: 4, y: 4, z: 16 (z_hi: 4, z_lo: 4; z = z_hi * 4 + z_lo), core: 2. Of those that a mesh axis runs over, the one named last changes fastest.
Arguments:
- streams: bfloat16 [5, 8192, 8192], P(None, 'seq', 'chan'), may hold values from -6 to 6
- short_filter: bfloat16 [7, 8192], P(None, 'chan'), may hold values from -2 to 2
- long_filter: bfloat16 [128, 8192], P(None, 'chan'), may hold values from -0.5 to 0.5
- edit_table: bfloat16 [64, 8, 8192], P('seq', None, 'chan'), may hold values from -0.25 to 0.25
- edit_bias: float32 [64, 4], replicated, may hold values from -8 to 8
- seq_tiles: int32 [4], replicated, may hold values from 1 to 32, 64 in all
- seq_tenant: int32 [4], replicated, may hold values from 0 to 63
Outputs:
- edited: bfloat16 [8192, 8192], P('seq', 'chan')
The draws below stay inside these ranges and needn't reach their ends.
Inputs may be any that keep to these rules, and one draw needn't show every extreme that they name: `seq_tiles`: each sequence fills whole tiles; the sequences fill all 64 tiles in order and the longest has 32.
All inputs are finite; a program needn't handle non-finite values.
Results may differ from the reference program's by a relative error of at most 0.013.
Values may be sent and summed in bfloat16 or wider, within the bound.
No kernel may reach another device: no remote copies, remote signals or barrier semaphores. Data moves between devices by JAX's collectives and lax.ppermute only.
A program may use at most 64 MiB of HBM per device.

```python
import math
import jax
import jax.numpy as jnp
import numpy as np
from jax import lax

D = 8192
TILE_ROWS = 128
SHORT_TAPS = 7
LONG_TAPS = 128
SEQS = 4
EDIT_RANK = 4
TENANTS = 64
TOKENS = 8192
TILES = 64


def with_ends(result, key, smallest, high):
    shape = result.shape
    index_at = [jax.random.randint(jax.random.fold_in(key, axis), (), 0, shape[axis]) for axis in range(len(shape))]
    result = result.at[tuple(index_at)].set(smallest)
    longest = shape.index(max(shape))
    index_at[longest] = (index_at[longest] + 1) % shape[longest]
    return result.at[tuple(index_at)].set(high)


def steps_of(stream_key, dims, cuts, low, top_value):
    factor_of = 1.0
    for axis_at, shards_of in cuts:
        draws = jax.random.uniform(jax.random.fold_in(jax.random.fold_in(stream_key, 6), axis_at), (shards_of,), jnp.float32, low / len(cuts), top_value / len(cuts))
        factor_of = factor_of * jnp.repeat(jnp.exp(draws), dims[axis_at] // shards_of).reshape((-1,) + (1,) * (len(dims) - 1 - axis_at))
    return factor_of


def split_up(count, total, limit, slope):
    portions = [(1 << 20) // math.isqrt(rank ** slope) + 1 for rank in range(2, count + 1)]
    rest, given = total - limit - (count - 1), [1] * (count - 1)
    while rest > 0:
        candidates = [i for i in range(count - 1) if given[i] < limit]
        pool, budget = sum([portions[i] for i in candidates]), rest
        for i in candidates:
            more = min(limit - given[i], max(1, budget * portions[i] // pool), rest)
            given[i] = given[i] + more
            rest = rest - more
    return np.array([limit] + given)


def ragged_sizes(rng, count, total, bound, skew):
    if count == 2:
        one = jax.random.randint(rng, (), max(1, total - bound), min(bound, total - 1) + 1)
        return jnp.stack([one, total - one])
    sizes = jnp.asarray(split_up(count, total, bound, skew), jnp.int32)
    twos = (count - 1) // 2
    donor, sink = sizes[1:1 + 2 * twos:2], sizes[2:2 + 2 * twos:2]
    room = jnp.minimum(donor - 1, bound - sink)
    passed = jax.random.randint(jax.random.fold_in(rng, 1), (twos,), 0, 1 << 20) % (room + 1)
    sizes = sizes.at[1:1 + 2 * twos:2].set(donor - passed).at[2:2 + 2 * twos:2].set(sink + passed)
    return sizes[jax.random.permutation(jax.random.fold_in(rng, 2), count)]


def bell_draw(stream_key, dims, deviation, bound, shards=(), held_as=jnp.bfloat16):
    entries = deviation * jax.random.normal(stream_key, dims, jnp.float32)
    if shards:
        entries = entries * steps_of(stream_key, dims, shards, -0.22, 0.18)
    return jnp.clip(entries, -bound, bound).astype(held_as)


def setup_inputs(seed: int = 0) -> dict:
    arg_keys = jax.random.split(jax.random.key(seed), 8)
    return {
        "streams": bell_draw(arg_keys[0], (5, TOKENS, D), 1.0, 6.0, ((1, 32), (2, 16))),
        "short_filter": bell_draw(arg_keys[1], (SHORT_TAPS, D), SHORT_TAPS ** -0.5, 2.0, ((1, 16),)),
        "long_filter": bell_draw(arg_keys[2], (LONG_TAPS, D), LONG_TAPS ** -0.5, 0.5, ((1, 16),)),
        "edit_table": bell_draw(arg_keys[3], (TENANTS, 2 * EDIT_RANK, D), (D // 16) ** -0.5, 0.25, ((0, 32), (2, 16))),
        "edit_bias": bell_draw(arg_keys[4], (TENANTS, EDIT_RANK), 2.0, 8.0, (), jnp.float32),
        "seq_tiles": ragged_sizes(arg_keys[5], SEQS, TILES, TILES // 2, 2).astype(jnp.int32),
        "seq_tenant": with_ends(jax.random.randint(arg_keys[6], (SEQS,), 0, TENANTS), jax.random.fold_in(arg_keys[6], 1), 0, TENANTS - 1).astype(jnp.int32),
    }


def tile_layout(seq_tiles):
    seq_ends = jnp.cumsum(seq_tiles).astype(jnp.int32)
    tile_ids = jnp.arange(TILES, dtype=jnp.int32)
    seq_of = jnp.sum((seq_ends[None, :] <= tile_ids[:, None]).astype(jnp.int32), axis=1).astype(jnp.int32)
    starts = (tile_ids == 0) | jnp.any(seq_ends[None, :] == tile_ids[:, None], axis=1)
    return seq_of, starts


def masked_conv(field, starts, taps_filter):
    width = field.shape[1]
    reach = taps_filter.shape[0]
    tiles = field.reshape(TILES, TILE_ROWS, width)
    trailing = tiles[:, TILE_ROWS - (reach - 1):, :]
    earlier = jnp.concatenate([jnp.zeros((1, reach - 1, width), field.dtype), trailing[:-1]], axis=0)
    earlier = jnp.where(starts[:, None, None], jnp.zeros_like(earlier), earlier)
    window = jnp.concatenate([earlier, tiles], axis=1)

    def add_tap(offset, total):
        rows = lax.dynamic_slice_in_dim(window, reach - 1 - offset, TILE_ROWS, 1)
        return total + rows * lax.dynamic_index_in_dim(taps_filter, offset, 0, keepdims=False)

    total = lax.fori_loop(0, reach, add_tap, jnp.zeros((TILES, TILE_ROWS, width), jnp.float32))
    return total.reshape(TILES * TILE_ROWS, width)


def reference(streams, short_filter, long_filter, edit_table, edit_bias, seq_tiles, seq_tenant):
    seq_of, starts = tile_layout(seq_tiles)
    first_gate = streams[0].astype(jnp.float32)
    first_key = streams[1].astype(jnp.float32)
    first_value = streams[2].astype(jnp.float32)
    second_gate = streams[3].astype(jnp.float32)
    second_key = streams[4].astype(jnp.float32)
    gated = (first_key * first_value).astype(jnp.bfloat16)
    short_out = masked_conv(gated.astype(jnp.float32), starts, short_filter.astype(jnp.float32))
    mixed = (first_gate * short_out).astype(jnp.bfloat16)
    carried = (second_key * mixed.astype(jnp.float32)).astype(jnp.bfloat16)
    long_out = masked_conv(carried.astype(jnp.float32), starts, long_filter.astype(jnp.float32))
    hidden = (second_gate * long_out).astype(jnp.bfloat16)
    tok_seq = jnp.repeat(seq_of, TILE_ROWS)
    seq_onehot = (tok_seq[:, None] == jnp.arange(SEQS, dtype=jnp.int32)[None, :]).astype(jnp.float32)
    chosen = edit_table[seq_tenant]
    projected = jnp.dot(hidden, chosen.reshape(SEQS * 2 * EDIT_RANK, D).T, preferred_element_type=jnp.float32)
    projected = projected.reshape(TOKENS, SEQS, 2 * EDIT_RANK)
    selected = jnp.sum(projected * seq_onehot[:, :, None], axis=1)
    bias_tok = jnp.dot(seq_onehot, edit_bias[seq_tenant], precision=lax.Precision.HIGHEST)
    coefficient = selected[:, EDIT_RANK:] - selected[:, :EDIT_RANK] + bias_tok
    spread = (seq_onehot[:, :, None] * coefficient[:, None, :]).reshape(TOKENS, SEQS * EDIT_RANK)
    rows_r = chosen[:, :EDIT_RANK, :].reshape(SEQS * EDIT_RANK, D).astype(jnp.float32)
    change = jnp.dot(spread, rows_r, precision=lax.Precision.HIGHEST)
    return (hidden.astype(jnp.float32) + change).astype(jnp.bfloat16)
```

```python
import jax
import jax.numpy as jnp
from jax import lax
from jax.sharding import PartitionSpec as P

TILE_ROWS = 128
SEQS = 4


def from_behind(block, axis, distance):
    devices = range(lax.axis_size(axis))
    route = [(i - distance, i) for i in devices if i - distance in devices]
    return lax.ppermute(block, axis, route)


def xor_sum(block, axis):
    size = lax.axis_size(axis)
    step = 1
    while step < size:
        route = [(i, i ^ step) for i in range(size)]
        block = block + lax.ppermute(block, axis, route)
        step *= 2
    return block


def a2a_sum(block, axis):
    size = lax.axis_size(axis)
    copies = jnp.broadcast_to(block[None], (size,) + block.shape)
    return jnp.sum(lax.all_to_all(copies, axis, 0, 0, tiled=False), axis=0)


def depth_conv(window, taps_filter):
    width = window.shape[-1]
    kernel = taps_filter[::-1][:, None, :]
    return lax.conv_general_dilated(
        window,
        kernel,
        (1,),
        "VALID",
        dimension_numbers=("NWC", "WIO", "NWC"),
        feature_group_count=width,
        preferred_element_type=jnp.float32,
    )


def on_device(streams, short_filter, long_filter, edit_table, edit_bias, seq_tiles, seq_tenant):
    rows_here = streams.shape[1]
    width = streams.shape[2]
    short_reach = short_filter.shape[0]
    long_reach = long_filter.shape[0]
    tile_count = rows_here // TILE_ROWS
    me = lax.axis_index("seq")
    seq_ends = jnp.cumsum(seq_tiles)
    tile_ids = me * tile_count + jnp.arange(tile_count, dtype=jnp.int32)
    seq_of = jnp.sum((seq_ends[None, :] <= tile_ids[:, None]).astype(jnp.int32), axis=1)
    starts = (tile_ids == 0) | jnp.any(seq_ends[None, :] == tile_ids[:, None], axis=1)

    held = edit_table.shape[0]
    owner_slot = seq_tenant - me * held
    owned = (owner_slot >= 0) & (owner_slot < held)
    local_rows = jnp.take(edit_table, jnp.clip(owner_slot, 0, held - 1), axis=0)
    local_rows = jnp.where(owned[:, None, None], local_rows, jnp.zeros_like(local_rows))
    chosen = xor_sum(local_rows, "seq")

    first_gate = streams[0].astype(jnp.float32)
    second_gate = streams[3].astype(jnp.float32)
    second_key = streams[4].astype(jnp.float32)
    gated = (streams[1].astype(jnp.float32) * streams[2].astype(jnp.float32)).astype(jnp.bfloat16)
    g_tiles = gated.reshape(tile_count, TILE_ROWS, width)

    def short_window(tile, earlier):
        earlier = jnp.where(starts[tile], jnp.zeros_like(earlier), earlier)
        return jnp.concatenate([earlier, g_tiles[tile]], axis=0)

    def carried_of(tile, short_out):
        rows = slice(tile * TILE_ROWS, (tile + 1) * TILE_ROWS)
        mixed = (first_gate[rows] * short_out).astype(jnp.bfloat16)
        return (second_key[rows] * mixed.astype(jnp.float32)).astype(jnp.bfloat16)

    later = [
        short_window(tile, g_tiles[tile - 1, TILE_ROWS - (short_reach - 1) :])
        for tile in range(1, tile_count)
    ]
    later_out = depth_conv(jnp.stack(later), short_filter)
    carried_later = [carried_of(tile, later_out[tile - 1]) for tile in range(1, tile_count)]

    border = jnp.concatenate(
        [gated[rows_here - (short_reach - 1) :], carried_later[-1][TILE_ROWS - (long_reach - 1) :]],
        axis=0,
    )
    border = from_behind(border, "seq", 1)
    short_border = border[: short_reach - 1]
    long_border = border[short_reach - 1 :]

    first_out = depth_conv(short_window(0, short_border)[None], short_filter)[0]
    carried = [carried_of(0, first_out)] + carried_later

    long_windows = []
    for tile in range(tile_count):
        earlier = long_border if tile == 0 else carried[tile - 1][TILE_ROWS - (long_reach - 1) :]
        earlier = jnp.where(starts[tile], jnp.zeros_like(earlier), earlier)
        long_windows.append(jnp.concatenate([earlier, carried[tile]], axis=0))
    long_out = depth_conv(jnp.stack(long_windows), long_filter)
    hidden = (second_gate.reshape(tile_count, TILE_ROWS, width) * long_out).astype(jnp.bfloat16)

    rows_per = edit_table.shape[1]
    rank = rows_per // 2
    tile_rows = jnp.take(chosen, seq_of, axis=0)
    projected = jnp.einsum(
        "tnc,trc->tnr", hidden, tile_rows, preferred_element_type=jnp.float32
    )
    partial = projected[..., rank:] - projected[..., :rank]
    summed = a2a_sum(partial, "chan")
    bias_tile = jnp.take(jnp.take(edit_bias, seq_tenant, axis=0), seq_of, axis=0)
    coefficient = summed + bias_tile[:, None, :]
    rows_r = tile_rows[:, :rank, :].astype(jnp.float32)
    total = hidden.astype(jnp.float32)
    for r in range(rank):
        total = total + coefficient[:, :, r : r + 1] * rows_r[:, r : r + 1, :]
    return total.astype(jnp.bfloat16).reshape(rows_here, width)


def solution(mesh):
    in_specs = (
        P(None, "seq", "chan"),
        P(None, "chan"),
        P(None, "chan"),
        P("seq", None, "chan"),
        P(),
        P(),
        P(),
    )
    out_specs = P("seq", "chan")
    return jax.shard_map(
        on_device, mesh=mesh, in_specs=in_specs, out_specs=out_specs, check_vma=False
    )
```

```python
import jax
import jax.numpy as jnp
from jax import lax
from jax.sharding import Mesh, PartitionSpec as P

TILE_ROWS = 128
SEQS = 4


SEQ = ("y", "near")
GROUP = 8


def shifted(block, distance):
    size = lax.axis_size(SEQ)
    return lax.ppermute(block, SEQ, [(i, (i + distance) % size) for i in range(size)])


def a2a_sum(block, axis):
    size = lax.axis_size(axis)
    copies = jnp.broadcast_to(block[None], (size,) + block.shape)
    return jnp.sum(lax.all_to_all(copies, axis, 0, 0, tiled=False), axis=0)


def depth_conv(window, taps_filter):
    width = window.shape[-1]
    kernel = taps_filter[::-1][:, None, :]
    return lax.conv_general_dilated(
        window,
        kernel,
        (1,),
        "VALID",
        dimension_numbers=("NWC", "WIO", "NWC"),
        feature_group_count=width,
        preferred_element_type=jnp.float32,
    )


def on_device(streams, short_filter, long_filter, edit_table, edit_bias, seq_tiles, seq_tenant):
    rows_here = streams.shape[1]
    width = streams.shape[2]
    short_reach = short_filter.shape[0]
    long_reach = long_filter.shape[0]
    tile_count = rows_here // TILE_ROWS
    me = lax.axis_index(SEQ)
    seq_ends = jnp.cumsum(seq_tiles)
    tile_ids = me * tile_count + jnp.arange(tile_count, dtype=jnp.int32)
    seq_of = jnp.sum((seq_ends[None, :] <= tile_ids[:, None]).astype(jnp.int32), axis=1)
    starts = (tile_ids == 0) | jnp.any(seq_ends[None, :] == tile_ids[:, None], axis=1)

    held = edit_table.shape[0]
    owner_slot = seq_tenant - me * held
    owned = (owner_slot >= 0) & (owner_slot < held)
    local_rows = jnp.take(edit_table, jnp.clip(owner_slot, 0, held - 1), axis=0)
    local_rows = jnp.where(owned[:, None, None], local_rows, jnp.zeros_like(local_rows))
    partial_rows = a2a_sum(local_rows, "y")

    first_gate = streams[0].astype(jnp.float32)
    second_gate = streams[3].astype(jnp.float32)
    second_key = streams[4].astype(jnp.float32)
    gated = (streams[1].astype(jnp.float32) * streams[2].astype(jnp.float32)).astype(jnp.bfloat16)
    g_tiles = gated.reshape(tile_count, TILE_ROWS, width)

    def short_window(tile, earlier):
        earlier = jnp.where(starts[tile], jnp.zeros_like(earlier), earlier)
        return jnp.concatenate([earlier, g_tiles[tile]], axis=0)

    def carried_of(tile, short_out):
        rows = slice(tile * TILE_ROWS, (tile + 1) * TILE_ROWS)
        mixed = (first_gate[rows] * short_out).astype(jnp.bfloat16)
        return (second_key[rows] * mixed.astype(jnp.float32)).astype(jnp.bfloat16)

    later = [
        short_window(tile, g_tiles[tile - 1, TILE_ROWS - (short_reach - 1) :])
        for tile in range(1, tile_count)
    ]
    later_out = depth_conv(jnp.stack(later), short_filter)
    carried_later = [carried_of(tile, later_out[tile - 1]) for tile in range(1, tile_count)]

    border = jnp.concatenate(
        [gated[rows_here - (short_reach - 1) :], carried_later[-1][TILE_ROWS - (long_reach - 1) :]],
        axis=0,
    )
    row_count = partial_rows.shape[0] * partial_rows.shape[1]
    sent = jnp.concatenate([border, partial_rows.reshape(row_count, width)], axis=0)
    sent = shifted(sent, 1)
    short_border = sent[: short_reach - 1]
    long_border = sent[short_reach - 1 : border.shape[0]]
    chosen = partial_rows + sent[border.shape[0] :].reshape(partial_rows.shape)
    distance = 2
    while distance < GROUP:
        chosen = chosen + shifted(chosen, distance)
        distance *= 2

    first_out = depth_conv(short_window(0, short_border)[None], short_filter)[0]
    carried = [carried_of(0, first_out)] + carried_later

    long_windows = []
    for tile in range(tile_count):
        earlier = long_border if tile == 0 else carried[tile - 1][TILE_ROWS - (long_reach - 1) :]
        earlier = jnp.where(starts[tile], jnp.zeros_like(earlier), earlier)
        long_windows.append(jnp.concatenate([earlier, carried[tile]], axis=0))
    long_out = depth_conv(jnp.stack(long_windows), long_filter)
    hidden = (second_gate.reshape(tile_count, TILE_ROWS, width) * long_out).astype(jnp.bfloat16)

    rows_per = edit_table.shape[1]
    rank = rows_per // 2
    tile_rows = jnp.take(chosen, seq_of, axis=0)
    projected = jnp.einsum(
        "tnc,trc->tnr", hidden, tile_rows, preferred_element_type=jnp.float32
    )
    partial = projected[..., rank:] - projected[..., :rank]
    summed = a2a_sum(partial, "chan")
    bias_tile = jnp.take(jnp.take(edit_bias, seq_tenant, axis=0), seq_of, axis=0)
    coefficient = summed + bias_tile[:, None, :]
    rows_r = tile_rows[:, :rank, :].astype(jnp.float32)
    total = hidden.astype(jnp.float32)
    for r in range(rank):
        total = total + coefficient[:, :, r : r + 1] * rows_r[:, r : r + 1, :]
    return total.astype(jnp.bfloat16).reshape(rows_here, width)


def solution(mesh):
    devices = mesh.devices.reshape(mesh.shape["seq"] // GROUP, GROUP, mesh.shape["chan"])
    split_mesh = Mesh(devices, ("y", "near", "chan"))
    in_specs = (
        P(None, SEQ, "chan"),
        P(None, "chan"),
        P(None, "chan"),
        P(SEQ, None, "chan"),
        P(),
        P(),
        P(),
    )
    out_specs = P(SEQ, "chan")
    return jax.shard_map(
        on_device, mesh=split_mesh, in_specs=in_specs, out_specs=out_specs, check_vma=False
    )
```

```python
import jax
import jax.numpy as jnp
from jax import lax
from jax.sharding import Mesh, PartitionSpec as P

TILE_ROWS = 128
SEQS = 4


SEQ = ("y", "zh", "core")


def shifted(block, distance):
    size = lax.axis_size(SEQ)
    return lax.ppermute(block, SEQ, [(i, (i + distance) % size) for i in range(size)])


def a2a_sum(block, axis):
    size = lax.axis_size(axis)
    copies = jnp.broadcast_to(block[None], (size,) + block.shape)
    return jnp.sum(lax.all_to_all(copies, axis, 0, 0, tiled=False), axis=0)


def depth_conv(window, taps_filter):
    width = window.shape[-1]
    kernel = taps_filter[::-1][:, None, :]
    return lax.conv_general_dilated(
        window,
        kernel,
        (1,),
        "VALID",
        dimension_numbers=("NWC", "WIO", "NWC"),
        feature_group_count=width,
        preferred_element_type=jnp.float32,
    )


def on_device(streams, short_filter, long_filter, edit_table, edit_bias, seq_tiles, seq_tenant):
    rows_here = streams.shape[1]
    width = streams.shape[2]
    short_reach = short_filter.shape[0]
    long_reach = long_filter.shape[0]
    tile_count = rows_here // TILE_ROWS
    me = lax.axis_index(SEQ)
    seq_ends = jnp.cumsum(seq_tiles)
    tile_ids = me * tile_count + jnp.arange(tile_count, dtype=jnp.int32)
    seq_of = jnp.sum((seq_ends[None, :] <= tile_ids[:, None]).astype(jnp.int32), axis=1)
    starts = (tile_ids == 0) | jnp.any(seq_ends[None, :] == tile_ids[:, None], axis=1)

    held = edit_table.shape[0]
    owner_slot = seq_tenant - me * held
    owned = (owner_slot >= 0) & (owner_slot < held)
    local_rows = jnp.take(edit_table, jnp.clip(owner_slot, 0, held - 1), axis=0)
    local_rows = jnp.where(owned[:, None, None], local_rows, jnp.zeros_like(local_rows))
    partial_rows = a2a_sum(local_rows, "y")

    first_gate = streams[0].astype(jnp.float32)
    second_gate = streams[3].astype(jnp.float32)
    second_key = streams[4].astype(jnp.float32)
    gated = (streams[1].astype(jnp.float32) * streams[2].astype(jnp.float32)).astype(jnp.bfloat16)
    g_tiles = gated.reshape(tile_count, TILE_ROWS, width)

    def short_window(tile, earlier):
        earlier = jnp.where(starts[tile], jnp.zeros_like(earlier), earlier)
        return jnp.concatenate([earlier, g_tiles[tile]], axis=0)

    def carried_of(tile, short_out):
        rows = slice(tile * TILE_ROWS, (tile + 1) * TILE_ROWS)
        mixed = (first_gate[rows] * short_out).astype(jnp.bfloat16)
        return (second_key[rows] * mixed.astype(jnp.float32)).astype(jnp.bfloat16)

    later = [
        short_window(tile, g_tiles[tile - 1, TILE_ROWS - (short_reach - 1) :])
        for tile in range(1, tile_count)
    ]
    later_out = depth_conv(jnp.stack(later), short_filter)
    carried_later = [carried_of(tile, later_out[tile - 1]) for tile in range(1, tile_count)]

    border = jnp.concatenate(
        [gated[rows_here - (short_reach - 1) :], carried_later[-1][TILE_ROWS - (long_reach - 1) :]],
        axis=0,
    )
    row_count = partial_rows.shape[0] * partial_rows.shape[1]
    sent = jnp.concatenate([border, partial_rows.reshape(row_count, width)], axis=0)
    sent = shifted(sent, 1)
    short_border = sent[: short_reach - 1]
    long_border = sent[short_reach - 1 : border.shape[0]]
    chosen = partial_rows + sent[border.shape[0] :].reshape(partial_rows.shape)
    chosen = a2a_sum(chosen, "zh")

    first_out = depth_conv(short_window(0, short_border)[None], short_filter)[0]
    carried = [carried_of(0, first_out)] + carried_later

    long_windows = []
    for tile in range(tile_count):
        earlier = long_border if tile == 0 else carried[tile - 1][TILE_ROWS - (long_reach - 1) :]
        earlier = jnp.where(starts[tile], jnp.zeros_like(earlier), earlier)
        long_windows.append(jnp.concatenate([earlier, carried[tile]], axis=0))
    long_out = depth_conv(jnp.stack(long_windows), long_filter)
    hidden = (second_gate.reshape(tile_count, TILE_ROWS, width) * long_out).astype(jnp.bfloat16)

    rows_per = edit_table.shape[1]
    rank = rows_per // 2
    tile_rows = jnp.take(chosen, seq_of, axis=0)
    projected = jnp.einsum(
        "tnc,trc->tnr", hidden, tile_rows, preferred_element_type=jnp.float32
    )
    partial = projected[..., rank:] - projected[..., :rank]
    summed = a2a_sum(partial, "chan")
    bias_tile = jnp.take(jnp.take(edit_bias, seq_tenant, axis=0), seq_of, axis=0)
    coefficient = summed + bias_tile[:, None, :]
    rows_r = tile_rows[:, :rank, :].astype(jnp.float32)
    total = hidden.astype(jnp.float32)
    for r in range(rank):
        total = total + coefficient[:, :, r : r + 1] * rows_r[:, r : r + 1, :]
    return total.astype(jnp.bfloat16).reshape(rows_here, width)


def solution(mesh):
    devices = mesh.devices.reshape(mesh.shape["seq"] // 8, 4, 2, mesh.shape["chan"])
    split_mesh = Mesh(devices, ("y", "zh", "core", "chan"))
    in_specs = (
        P(None, SEQ, "chan"),
        P(None, "chan"),
        P(None, "chan"),
        P(SEQ, None, "chan"),
        P(),
        P(),
        P(),
    )
    out_specs = P(SEQ, "chan")
    return jax.shard_map(
        on_device, mesh=split_mesh, in_specs=in_specs, out_specs=out_specs, check_vma=False
    )
```

```python
import jax
import jax.numpy as jnp
from jax import lax
from jax.sharding import Mesh, PartitionSpec as P

TILE_ROWS = 128
SEQS = 4


SEQ = ("y", "zh", "core")


def shifted(block, distance):
    size = lax.axis_size(SEQ)
    return lax.ppermute(block, SEQ, [(i, (i + distance) % size) for i in range(size)])


def a2a_sum(block, axis):
    size = lax.axis_size(axis)
    copies = jnp.broadcast_to(block[None], (size,) + block.shape)
    return jnp.sum(lax.all_to_all(copies, axis, 0, 0, tiled=False), axis=0)


def depth_conv(window, taps_filter):
    width = window.shape[-1]
    kernel = taps_filter[::-1][:, None, :]
    return lax.conv_general_dilated(
        window,
        kernel,
        (1,),
        "VALID",
        dimension_numbers=("NWC", "WIO", "NWC"),
        feature_group_count=width,
        preferred_element_type=jnp.float32,
    )


def on_device(streams, short_filter, long_filter, edit_table, edit_bias, seq_tiles, seq_tenant):
    rows_here = streams.shape[1]
    width = streams.shape[2]
    short_reach = short_filter.shape[0]
    long_reach = long_filter.shape[0]
    tile_count = rows_here // TILE_ROWS
    me = lax.axis_index(SEQ)
    seq_ends = jnp.cumsum(seq_tiles)
    tile_ids = me * tile_count + jnp.arange(tile_count, dtype=jnp.int32)
    seq_of = jnp.sum((seq_ends[None, :] <= tile_ids[:, None]).astype(jnp.int32), axis=1)
    starts = (tile_ids == 0) | jnp.any(seq_ends[None, :] == tile_ids[:, None], axis=1)

    held = edit_table.shape[0]
    owner_slot = seq_tenant - me * held
    picked = []
    for s in range(SEQS):
        rows = jnp.zeros_like(edit_table[0])
        for slot in range(held):
            rows = jnp.where(owner_slot[s] == slot, edit_table[slot], rows)
        picked.append(rows)
    local_rows = jnp.stack(picked)
    partial_rows = a2a_sum(local_rows, "y")

    first_gate = streams[0].astype(jnp.float32)
    second_gate = streams[3].astype(jnp.float32)
    second_key = streams[4].astype(jnp.float32)
    gated = (streams[1].astype(jnp.float32) * streams[2].astype(jnp.float32)).astype(jnp.bfloat16)
    g_tiles = gated.reshape(tile_count, TILE_ROWS, width)

    def short_window(tile, earlier):
        earlier = jnp.where(starts[tile], jnp.zeros_like(earlier), earlier)
        return jnp.concatenate([earlier, g_tiles[tile]], axis=0)

    def carried_of(tile, short_out):
        rows = slice(tile * TILE_ROWS, (tile + 1) * TILE_ROWS)
        mixed = (first_gate[rows] * short_out).astype(jnp.bfloat16)
        return (second_key[rows] * mixed.astype(jnp.float32)).astype(jnp.bfloat16)

    later = [
        short_window(tile, g_tiles[tile - 1, TILE_ROWS - (short_reach - 1) :])
        for tile in range(1, tile_count)
    ]
    later_out = depth_conv(jnp.stack(later), short_filter)
    carried_later = [carried_of(tile, later_out[tile - 1]) for tile in range(1, tile_count)]

    border = jnp.concatenate(
        [gated[rows_here - (short_reach - 1) :], carried_later[-1][TILE_ROWS - (long_reach - 1) :]],
        axis=0,
    )
    row_count = partial_rows.shape[0] * partial_rows.shape[1]
    sent = jnp.concatenate([border, partial_rows.reshape(row_count, width)], axis=0)
    sent = shifted(sent, 1)
    short_border = sent[: short_reach - 1]
    long_border = sent[short_reach - 1 : border.shape[0]]
    chosen = partial_rows + sent[border.shape[0] :].reshape(partial_rows.shape)
    zh_size = lax.axis_size("zh")
    peer = me + (jnp.arange(zh_size, dtype=jnp.int32) - lax.axis_index("zh")) * lax.axis_size("core")
    peer_tiles = peer[:, None] * tile_count + jnp.arange(tile_count, dtype=jnp.int32)[None, :]
    peer_seq = jnp.sum((seq_ends[None, None, :] <= peer_tiles[:, :, None]).astype(jnp.int32), axis=2)
    outgoing = jnp.zeros((zh_size, tile_count) + chosen.shape[1:], chosen.dtype)
    for s in range(SEQS):
        outgoing = jnp.where((peer_seq == s)[:, :, None, None], chosen[s], outgoing)
    tile_rows = jnp.sum(lax.all_to_all(outgoing, "zh", 0, 0, tiled=False), axis=0)

    first_out = depth_conv(short_window(0, short_border)[None], short_filter)[0]
    carried = [carried_of(0, first_out)] + carried_later

    long_windows = []
    for tile in range(tile_count):
        earlier = long_border if tile == 0 else carried[tile - 1][TILE_ROWS - (long_reach - 1) :]
        earlier = jnp.where(starts[tile], jnp.zeros_like(earlier), earlier)
        long_windows.append(jnp.concatenate([earlier, carried[tile]], axis=0))
    long_out = depth_conv(jnp.stack(long_windows), long_filter)
    hidden = (second_gate.reshape(tile_count, TILE_ROWS, width) * long_out).astype(jnp.bfloat16)

    rows_per = edit_table.shape[1]
    rank = rows_per // 2
    projected = jnp.einsum(
        "tnc,trc->tnr", hidden, tile_rows, preferred_element_type=jnp.float32
    )
    partial = projected[..., rank:] - projected[..., :rank]
    summed = a2a_sum(partial, "chan")
    bias_tile = jnp.take(jnp.take(edit_bias, seq_tenant, axis=0), seq_of, axis=0)
    coefficient = summed + bias_tile[:, None, :]
    rows_r = tile_rows[:, :rank, :].astype(jnp.float32)
    total = hidden.astype(jnp.float32)
    for r in range(rank):
        total = total + coefficient[:, :, r : r + 1] * rows_r[:, r : r + 1, :]
    return total.astype(jnp.bfloat16).reshape(rows_here, width)


def solution(mesh):
    devices = mesh.devices.reshape(mesh.shape["seq"] // 8, 4, 2, mesh.shape["chan"])
    split_mesh = Mesh(devices, ("y", "zh", "core", "chan"))
    in_specs = (
        P(None, SEQ, "chan"),
        P(None, "chan"),
        P(None, "chan"),
        P(SEQ, None, "chan"),
        P(),
        P(),
        P(),
    )
    out_specs = P(SEQ, "chan")
    return jax.shard_map(
        on_device, mesh=split_mesh, in_specs=in_specs, out_specs=out_specs, check_vma=False
    )
```

```python
import jax
import jax.numpy as jnp
from jax import lax
from jax.sharding import Mesh, PartitionSpec as P

TILE_ROWS = 128
SEQS = 4


SEQ = ("y", "zh", "core")


def shifted(block, distance):
    size = lax.axis_size(SEQ)
    return lax.ppermute(block, SEQ, [(i, (i + distance) % size) for i in range(size)])


def a2a_sum(block, axis):
    size = lax.axis_size(axis)
    copies = jnp.broadcast_to(block[None], (size,) + block.shape)
    return jnp.sum(lax.all_to_all(copies, axis, 0, 0, tiled=False), axis=0)


def depth_conv(window, taps_filter):
    width = window.shape[-1]
    kernel = taps_filter[::-1][:, None, :]
    return lax.conv_general_dilated(
        window,
        kernel,
        (1,),
        "VALID",
        dimension_numbers=("NWC", "WIO", "NWC"),
        feature_group_count=width,
        preferred_element_type=jnp.float32,
    )


def on_device(streams, short_filter, long_filter, edit_table, edit_bias, seq_tiles, seq_tenant):
    rows_here = streams.shape[1]
    width = streams.shape[2]
    short_reach = short_filter.shape[0]
    long_reach = long_filter.shape[0]
    tile_count = rows_here // TILE_ROWS
    me = lax.axis_index(SEQ)
    seq_ends = jnp.cumsum(seq_tiles)
    tile_ids = me * tile_count + jnp.arange(tile_count, dtype=jnp.int32)
    seq_of = jnp.sum((seq_ends[None, :] <= tile_ids[:, None]).astype(jnp.int32), axis=1)
    starts = (tile_ids == 0) | jnp.any(seq_ends[None, :] == tile_ids[:, None], axis=1)

    held = edit_table.shape[0]
    owner_slot = seq_tenant - me * held
    owned = (owner_slot >= 0) & (owner_slot < held)
    local_rows = jnp.take(edit_table, jnp.clip(owner_slot, 0, held - 1), axis=0)
    local_rows = jnp.where(owned[:, None, None], local_rows, jnp.zeros_like(local_rows))
    partial_rows = a2a_sum(local_rows, "y")

    first_gate = streams[0].astype(jnp.float32)
    second_gate = streams[3].astype(jnp.float32)
    second_key = streams[4].astype(jnp.float32)
    gated = (streams[1].astype(jnp.float32) * streams[2].astype(jnp.float32)).astype(jnp.bfloat16)
    g_tiles = gated.reshape(tile_count, TILE_ROWS, width)

    def short_window(tile, earlier):
        earlier = jnp.where(starts[tile], jnp.zeros_like(earlier), earlier)
        return jnp.concatenate([earlier, g_tiles[tile]], axis=0)

    def carried_of(tile, short_out):
        rows = slice(tile * TILE_ROWS, (tile + 1) * TILE_ROWS)
        mixed = (first_gate[rows] * short_out).astype(jnp.bfloat16)
        return (second_key[rows] * mixed.astype(jnp.float32)).astype(jnp.bfloat16)

    later = [
        short_window(tile, g_tiles[tile - 1, TILE_ROWS - (short_reach - 1) :])
        for tile in range(1, tile_count)
    ]
    later_out = depth_conv(jnp.stack(later), short_filter)
    carried_later = [carried_of(tile, later_out[tile - 1]) for tile in range(1, tile_count)]

    border = jnp.concatenate(
        [gated[rows_here - (short_reach - 1) :], carried_later[-1][TILE_ROWS - (long_reach - 1) :]],
        axis=0,
    )
    row_count = partial_rows.shape[0] * partial_rows.shape[1]
    sent = jnp.concatenate([border, partial_rows.reshape(row_count, width)], axis=0)
    sent = shifted(sent, 1)
    short_border = sent[: short_reach - 1]
    long_border = sent[short_reach - 1 : border.shape[0]]
    chosen = partial_rows + sent[border.shape[0] :].reshape(partial_rows.shape)
    zh_size = lax.axis_size("zh")
    peer = me + (jnp.arange(zh_size, dtype=jnp.int32) - lax.axis_index("zh")) * lax.axis_size("core")
    peer_tiles = peer[:, None] * tile_count + jnp.arange(tile_count, dtype=jnp.int32)[None, :]
    peer_seq = jnp.sum((seq_ends[None, None, :] <= peer_tiles[:, :, None]).astype(jnp.int32), axis=2)
    outgoing = jnp.zeros((zh_size, tile_count) + chosen.shape[1:], chosen.dtype)
    for s in range(SEQS):
        outgoing = jnp.where((peer_seq == s)[:, :, None, None], chosen[s], outgoing)
    tile_rows = jnp.sum(lax.all_to_all(outgoing, "zh", 0, 0, tiled=False), axis=0)

    first_out = depth_conv(short_window(0, short_border)[None], short_filter)[0]
    carried = [carried_of(0, first_out)] + carried_later

    long_windows = []
    for tile in range(tile_count):
        earlier = long_border if tile == 0 else carried[tile - 1][TILE_ROWS - (long_reach - 1) :]
        earlier = jnp.where(starts[tile], jnp.zeros_like(earlier), earlier)
        long_windows.append(jnp.concatenate([earlier, carried[tile]], axis=0))
    long_out = depth_conv(jnp.stack(long_windows), long_filter)
    hidden = (second_gate.reshape(tile_count, TILE_ROWS, width) * long_out).astype(jnp.bfloat16)

    rows_per = edit_table.shape[1]
    rank = rows_per // 2
    projected = jnp.einsum(
        "tnc,trc->tnr", hidden, tile_rows, preferred_element_type=jnp.float32
    )
    partial = projected[..., rank:] - projected[..., :rank]
    summed = a2a_sum(partial, "chan")
    bias_tile = jnp.take(jnp.take(edit_bias, seq_tenant, axis=0), seq_of, axis=0)
    coefficient = summed + bias_tile[:, None, :]
    rows_r = tile_rows[:, :rank, :].astype(jnp.float32)
    total = hidden.astype(jnp.float32)
    for r in range(rank):
        total = total + coefficient[:, :, r : r + 1] * rows_r[:, r : r + 1, :]
    return total.astype(jnp.bfloat16).reshape(rows_here, width)


def solution(mesh):
    devices = mesh.devices.reshape(mesh.shape["seq"] // 8, 4, 2, mesh.shape["chan"])
    split_mesh = Mesh(devices, ("y", "zh", "core", "chan"))
    in_specs = (
        P(None, SEQ, "chan"),
        P(None, "chan"),
        P(None, "chan"),
        P(SEQ, None, "chan"),
        P(),
        P(),
        P(),
    )
    out_specs = P(SEQ, "chan")
    return jax.shard_map(
        on_device, mesh=split_mesh, in_specs=in_specs, out_specs=out_specs, check_vma=False
    )
```

```python
import jax
import jax.numpy as jnp
from jax import lax
from jax.sharding import Mesh, PartitionSpec as P

TILE_ROWS = 128
SEQS = 4


SEQ = ("y", "zh", "core")


def shifted(block, distance):
    size = lax.axis_size(SEQ)
    return lax.ppermute(block, SEQ, [(i, (i + distance) % size) for i in range(size)])


def a2a_sum(block, axis):
    size = lax.axis_size(axis)
    copies = jnp.broadcast_to(block[None], (size,) + block.shape)
    return jnp.sum(lax.all_to_all(copies, axis, 0, 0, tiled=False), axis=0)


def depth_conv(window, taps_filter):
    width = window.shape[-1]
    kernel = taps_filter[::-1][:, None, :]
    return lax.conv_general_dilated(
        window,
        kernel,
        (1,),
        "VALID",
        dimension_numbers=("NWC", "WIO", "NWC"),
        feature_group_count=width,
        preferred_element_type=jnp.float32,
    )


def on_device(streams, short_filter, long_filter, edit_table, edit_bias, seq_tiles, seq_tenant):
    rows_here = streams.shape[1]
    width = streams.shape[2]
    short_reach = short_filter.shape[0]
    long_reach = long_filter.shape[0]
    tile_count = rows_here // TILE_ROWS
    me = lax.axis_index(SEQ)
    seq_ends = jnp.cumsum(seq_tiles)
    tile_ids = me * tile_count + jnp.arange(tile_count, dtype=jnp.int32)
    seq_of = jnp.sum((seq_ends[None, :] <= tile_ids[:, None]).astype(jnp.int32), axis=1)
    starts = (tile_ids == 0) | jnp.any(seq_ends[None, :] == tile_ids[:, None], axis=1)

    held = edit_table.shape[0]
    owner_slot = seq_tenant - me * held
    owned = (owner_slot >= 0) & (owner_slot < held)
    local_rows = jnp.take(edit_table, jnp.clip(owner_slot, 0, held - 1), axis=0)
    local_rows = jnp.where(owned[:, None, None], local_rows, jnp.zeros_like(local_rows))
    partial_rows = local_rows

    first_gate = streams[0].astype(jnp.float32)
    second_gate = streams[3].astype(jnp.float32)
    second_key = streams[4].astype(jnp.float32)
    gated = (streams[1].astype(jnp.float32) * streams[2].astype(jnp.float32)).astype(jnp.bfloat16)
    g_tiles = gated.reshape(tile_count, TILE_ROWS, width)

    def short_window(tile, earlier):
        earlier = jnp.where(starts[tile], jnp.zeros_like(earlier), earlier)
        return jnp.concatenate([earlier, g_tiles[tile]], axis=0)

    def carried_of(tile, short_out):
        rows = slice(tile * TILE_ROWS, (tile + 1) * TILE_ROWS)
        mixed = (first_gate[rows] * short_out).astype(jnp.bfloat16)
        return (second_key[rows] * mixed.astype(jnp.float32)).astype(jnp.bfloat16)

    later = [
        short_window(tile, g_tiles[tile - 1, TILE_ROWS - (short_reach - 1) :])
        for tile in range(1, tile_count)
    ]
    later_out = depth_conv(jnp.stack(later), short_filter)
    carried_later = [carried_of(tile, later_out[tile - 1]) for tile in range(1, tile_count)]

    border = jnp.concatenate(
        [gated[rows_here - (short_reach - 1) :], carried_later[-1][TILE_ROWS - (long_reach - 1) :]],
        axis=0,
    )
    row_count = partial_rows.shape[0] * partial_rows.shape[1]
    sent = jnp.concatenate([border, partial_rows.reshape(row_count, width)], axis=0)
    sent = shifted(sent, 1)
    short_border = sent[: short_reach - 1]
    long_border = sent[short_reach - 1 : border.shape[0]]
    chosen = a2a_sum(partial_rows + sent[border.shape[0] :].reshape(partial_rows.shape), "y")
    zh_size = lax.axis_size("zh")
    peer = me + (jnp.arange(zh_size, dtype=jnp.int32) - lax.axis_index("zh")) * lax.axis_size("core")
    peer_tiles = peer[:, None] * tile_count + jnp.arange(tile_count, dtype=jnp.int32)[None, :]
    peer_seq = jnp.sum((seq_ends[None, None, :] <= peer_tiles[:, :, None]).astype(jnp.int32), axis=2)
    outgoing = jnp.zeros((zh_size, tile_count) + chosen.shape[1:], chosen.dtype)
    for s in range(SEQS):
        outgoing = jnp.where((peer_seq == s)[:, :, None, None], chosen[s], outgoing)
    tile_rows = jnp.sum(lax.all_to_all(outgoing, "zh", 0, 0, tiled=False), axis=0)

    first_out = depth_conv(short_window(0, short_border)[None], short_filter)[0]
    carried = [carried_of(0, first_out)] + carried_later

    long_windows = []
    for tile in range(tile_count):
        earlier = long_border if tile == 0 else carried[tile - 1][TILE_ROWS - (long_reach - 1) :]
        earlier = jnp.where(starts[tile], jnp.zeros_like(earlier), earlier)
        long_windows.append(jnp.concatenate([earlier, carried[tile]], axis=0))
    long_out = depth_conv(jnp.stack(long_windows), long_filter)
    hidden = (second_gate.reshape(tile_count, TILE_ROWS, width) * long_out).astype(jnp.bfloat16)

    rows_per = edit_table.shape[1]
    rank = rows_per // 2
    projected = jnp.einsum(
        "tnc,trc->tnr", hidden, tile_rows, preferred_element_type=jnp.float32
    )
    partial = projected[..., rank:] - projected[..., :rank]
    summed = a2a_sum(partial, "chan")
    bias_tile = jnp.take(jnp.take(edit_bias, seq_tenant, axis=0), seq_of, axis=0)
    coefficient = summed + bias_tile[:, None, :]
    rows_r = tile_rows[:, :rank, :].astype(jnp.float32)
    total = hidden.astype(jnp.float32)
    for r in range(rank):
        total = total + coefficient[:, :, r : r + 1] * rows_r[:, r : r + 1, :]
    return total.astype(jnp.bfloat16).reshape(rows_here, width)


def solution(mesh):
    devices = mesh.devices.reshape(mesh.shape["seq"] // 8, 4, 2, mesh.shape["chan"])
    split_mesh = Mesh(devices, ("y", "zh", "core", "chan"))
    in_specs = (
        P(None, SEQ, "chan"),
        P(None, "chan"),
        P(None, "chan"),
        P(SEQ, None, "chan"),
        P(),
        P(),
        P(),
    )
    out_specs = P(SEQ, "chan")
    return jax.shard_map(
        on_device, mesh=split_mesh, in_specs=in_specs, out_specs=out_specs, check_vma=False
    )
```

```python
import jax
import jax.numpy as jnp
from jax import lax
from jax.sharding import Mesh, PartitionSpec as P

TILE_ROWS = 128
SEQS = 4


SEQ = ("y", "zh", "core")


def shifted(block, distance):
    size = lax.axis_size(SEQ)
    return lax.ppermute(block, SEQ, [(i, (i + distance) % size) for i in range(size)])


def a2a_sum(block, axis):
    size = lax.axis_size(axis)
    copies = jnp.broadcast_to(block[None], (size,) + block.shape)
    return jnp.sum(lax.all_to_all(copies, axis, 0, 0, tiled=False), axis=0)


def depth_conv(window, taps_filter):
    width = window.shape[-1]
    kernel = taps_filter[::-1][:, None, :]
    return lax.conv_general_dilated(
        window,
        kernel,
        (1,),
        "VALID",
        dimension_numbers=("NWC", "WIO", "NWC"),
        feature_group_count=width,
        preferred_element_type=jnp.float32,
    )


def on_device(streams, short_filter, long_filter, edit_table, edit_bias, seq_tiles, seq_tenant):
    rows_here = streams.shape[1]
    width = streams.shape[2]
    short_reach = short_filter.shape[0]
    long_reach = long_filter.shape[0]
    tile_count = rows_here // TILE_ROWS
    me = lax.axis_index(SEQ)
    seq_ends = jnp.cumsum(seq_tiles)
    tile_ids = me * tile_count + jnp.arange(tile_count, dtype=jnp.int32)
    seq_of = jnp.sum((seq_ends[None, :] <= tile_ids[:, None]).astype(jnp.int32), axis=1)
    starts = (tile_ids == 0) | jnp.any(seq_ends[None, :] == tile_ids[:, None], axis=1)

    held = edit_table.shape[0]
    owner_slot = seq_tenant - me * held
    owned = (owner_slot >= 0) & (owner_slot < held)
    local_rows = jnp.take(edit_table, jnp.clip(owner_slot, 0, held - 1), axis=0)
    local_rows = jnp.where(owned[:, None, None], local_rows, jnp.zeros_like(local_rows))
    partial_rows = local_rows

    first_gate = streams[0].astype(jnp.float32)
    second_gate = streams[3].astype(jnp.float32)
    second_key = streams[4].astype(jnp.float32)
    gated = (streams[1].astype(jnp.float32) * streams[2].astype(jnp.float32)).astype(jnp.bfloat16)
    g_tiles = gated.reshape(tile_count, TILE_ROWS, width)

    def short_window(tile, earlier):
        earlier = jnp.where(starts[tile], jnp.zeros_like(earlier), earlier)
        return jnp.concatenate([earlier, g_tiles[tile]], axis=0)

    def carried_of(tile, short_out):
        rows = slice(tile * TILE_ROWS, (tile + 1) * TILE_ROWS)
        mixed = (first_gate[rows] * short_out).astype(jnp.bfloat16)
        return (second_key[rows] * mixed.astype(jnp.float32)).astype(jnp.bfloat16)

    later = [
        short_window(tile, g_tiles[tile - 1, TILE_ROWS - (short_reach - 1) :])
        for tile in range(1, tile_count)
    ]
    later_out = depth_conv(jnp.stack(later), short_filter)
    carried_later = [carried_of(tile, later_out[tile - 1]) for tile in range(1, tile_count)]

    border = jnp.concatenate(
        [gated[rows_here - (short_reach - 1) :], carried_later[-1][TILE_ROWS - (long_reach - 1) :]],
        axis=0,
    )
    row_count = partial_rows.shape[0] * partial_rows.shape[1]
    sent = jnp.concatenate([border, partial_rows.reshape(row_count, width)], axis=0)
    sent = shifted(sent, 1)
    short_border = sent[: short_reach - 1]
    long_border = sent[short_reach - 1 : border.shape[0]]
    chosen = partial_rows + sent[border.shape[0] :].reshape(partial_rows.shape)
    zh_size = lax.axis_size(SEQ[:2])
    peer = jnp.arange(zh_size, dtype=jnp.int32) * lax.axis_size("core") + lax.axis_index("core")
    peer_tiles = peer[:, None] * tile_count + jnp.arange(tile_count, dtype=jnp.int32)[None, :]
    peer_seq = jnp.sum((seq_ends[None, None, :] <= peer_tiles[:, :, None]).astype(jnp.int32), axis=2)
    outgoing = jnp.zeros((zh_size, tile_count) + chosen.shape[1:], chosen.dtype)
    for s in range(SEQS):
        outgoing = jnp.where((peer_seq == s)[:, :, None, None], chosen[s], outgoing)
    tile_rows = jnp.sum(lax.all_to_all(outgoing, SEQ[:2], 0, 0, tiled=False), axis=0)

    first_out = depth_conv(short_window(0, short_border)[None], short_filter)[0]
    carried = [carried_of(0, first_out)] + carried_later

    long_windows = []
    for tile in range(tile_count):
        earlier = long_border if tile == 0 else carried[tile - 1][TILE_ROWS - (long_reach - 1) :]
        earlier = jnp.where(starts[tile], jnp.zeros_like(earlier), earlier)
        long_windows.append(jnp.concatenate([earlier, carried[tile]], axis=0))
    long_out = depth_conv(jnp.stack(long_windows), long_filter)
    hidden = (second_gate.reshape(tile_count, TILE_ROWS, width) * long_out).astype(jnp.bfloat16)

    rows_per = edit_table.shape[1]
    rank = rows_per // 2
    projected = jnp.einsum(
        "tnc,trc->tnr", hidden, tile_rows, preferred_element_type=jnp.float32
    )
    partial = projected[..., rank:] - projected[..., :rank]
    summed = a2a_sum(partial, "chan")
    bias_tile = jnp.take(jnp.take(edit_bias, seq_tenant, axis=0), seq_of, axis=0)
    coefficient = summed + bias_tile[:, None, :]
    rows_r = tile_rows[:, :rank, :].astype(jnp.float32)
    total = hidden.astype(jnp.float32)
    for r in range(rank):
        total = total + coefficient[:, :, r : r + 1] * rows_r[:, r : r + 1, :]
    return total.astype(jnp.bfloat16).reshape(rows_here, width)


def solution(mesh):
    devices = mesh.devices.reshape(mesh.shape["seq"] // 8, 4, 2, mesh.shape["chan"])
    split_mesh = Mesh(devices, ("y", "zh", "core", "chan"))
    in_specs = (
        P(None, SEQ, "chan"),
        P(None, "chan"),
        P(None, "chan"),
        P(SEQ, None, "chan"),
        P(),
        P(),
        P(),
    )
    out_specs = P(SEQ, "chan")
    return jax.shard_map(
        on_device, mesh=split_mesh, in_specs=in_specs, out_specs=out_specs, check_vma=False
    )
```

```python
import jax
import jax.numpy as jnp
from jax import lax
from jax.sharding import Mesh, PartitionSpec as P

TILE_ROWS = 128
SEQS = 4


SEQ = ("y", "zh", "core")


def shifted(block, distance):
    size = lax.axis_size(SEQ)
    return lax.ppermute(block, SEQ, [(i, (i + distance) % size) for i in range(size)])


def a2a_sum(block, axis):
    size = lax.axis_size(axis)
    copies = jnp.broadcast_to(block[None], (size,) + block.shape)
    return jnp.sum(lax.all_to_all(copies, axis, 0, 0, tiled=False), axis=0)


def depth_conv(window, taps_filter):
    width = window.shape[-1]
    kernel = taps_filter[::-1][:, None, :]
    return lax.conv_general_dilated(
        window,
        kernel,
        (1,),
        "VALID",
        dimension_numbers=("NWC", "WIO", "NWC"),
        feature_group_count=width,
        preferred_element_type=jnp.float32,
    )


def on_device(streams, short_filter, long_filter, edit_table, edit_bias, seq_tiles, seq_tenant):
    rows_here = streams.shape[1]
    width = streams.shape[2]
    short_reach = short_filter.shape[0]
    long_reach = long_filter.shape[0]
    tile_count = rows_here // TILE_ROWS
    me = lax.axis_index(SEQ)
    seq_ends = jnp.cumsum(seq_tiles)
    tile_ids = me * tile_count + jnp.arange(tile_count, dtype=jnp.int32)
    seq_of = jnp.sum((seq_ends[None, :] <= tile_ids[:, None]).astype(jnp.int32), axis=1)
    starts = (tile_ids == 0) | jnp.any(seq_ends[None, :] == tile_ids[:, None], axis=1)

    held = edit_table.shape[0]
    owner_slot = seq_tenant - me * held
    owned = (owner_slot >= 0) & (owner_slot < held)
    local_rows = jnp.take(edit_table, jnp.clip(owner_slot, 0, held - 1), axis=0)
    local_rows = jnp.where(owned[:, None, None], local_rows, jnp.zeros_like(local_rows))
    partial_rows = local_rows

    def gated_rows(begin, stop):
        key = streams[1, begin:stop].astype(jnp.float32)
        return (key * streams[2, begin:stop].astype(jnp.float32)).astype(jnp.bfloat16)

    def short_window(tile, earlier, own):
        earlier = jnp.where(starts[tile], jnp.zeros_like(earlier), earlier)
        return jnp.concatenate([earlier, own], axis=0)

    def carried_of(tile, window):
        short_out = depth_conv(window[None], short_filter)[0]
        rows = slice(tile * TILE_ROWS, (tile + 1) * TILE_ROWS)
        mixed = (streams[0, rows].astype(jnp.float32) * short_out).astype(jnp.bfloat16)
        return (streams[4, rows].astype(jnp.float32) * mixed.astype(jnp.float32)).astype(jnp.bfloat16)

    last = tile_count - 1
    last_window = gated_rows(last * TILE_ROWS - (short_reach - 1), rows_here)
    carried_last = carried_of(
        last, short_window(last, last_window[: short_reach - 1], last_window[short_reach - 1 :])
    )
    border = jnp.concatenate(
        [last_window[TILE_ROWS:], carried_last[TILE_ROWS - (long_reach - 1) :]], axis=0
    )
    row_count = partial_rows.shape[0] * partial_rows.shape[1]
    sent = jnp.concatenate([border, partial_rows.reshape(row_count, width)], axis=0)
    sent = shifted(sent, 1)
    short_border = sent[: short_reach - 1]
    long_border = sent[short_reach - 1 : border.shape[0]]
    chosen = partial_rows + sent[border.shape[0] :].reshape(partial_rows.shape)
    zh_size = lax.axis_size(SEQ[:2])
    peer = jnp.arange(zh_size, dtype=jnp.int32) * lax.axis_size("core") + lax.axis_index("core")
    peer_tiles = peer[:, None] * tile_count + jnp.arange(tile_count, dtype=jnp.int32)[None, :]
    peer_seq = jnp.sum((seq_ends[None, None, :] <= peer_tiles[:, :, None]).astype(jnp.int32), axis=2)
    outgoing = jnp.zeros((zh_size, tile_count) + chosen.shape[1:], chosen.dtype)
    for s in range(SEQS):
        outgoing = jnp.where((peer_seq == s)[:, :, None, None], chosen[s], outgoing)
    tile_rows = jnp.sum(lax.all_to_all(outgoing, SEQ[:2], 0, 0, tiled=False), axis=0)

    gated_first = gated_rows(0, last * TILE_ROWS)
    carried = []
    for tile in range(last):
        own = gated_first[tile * TILE_ROWS : (tile + 1) * TILE_ROWS]
        if tile == 0:
            earlier = short_border
        else:
            earlier = gated_first[tile * TILE_ROWS - (short_reach - 1) : tile * TILE_ROWS]
        carried.append(carried_of(tile, short_window(tile, earlier, own)))
    carried.append(carried_last)

    long_windows = []
    for tile in range(tile_count):
        earlier = long_border if tile == 0 else carried[tile - 1][TILE_ROWS - (long_reach - 1) :]
        earlier = jnp.where(starts[tile], jnp.zeros_like(earlier), earlier)
        long_windows.append(jnp.concatenate([earlier, carried[tile]], axis=0))
    long_out = depth_conv(jnp.stack(long_windows), long_filter)
    second_gate = streams[3].astype(jnp.float32).reshape(tile_count, TILE_ROWS, width)
    hidden = (second_gate * long_out).astype(jnp.bfloat16)

    rows_per = edit_table.shape[1]
    rank = rows_per // 2
    projected = jnp.einsum(
        "tnc,trc->tnr", hidden, tile_rows, preferred_element_type=jnp.float32
    )
    partial = projected[..., rank:] - projected[..., :rank]
    summed = a2a_sum(partial, "chan")
    bias_tile = jnp.take(jnp.take(edit_bias, seq_tenant, axis=0), seq_of, axis=0)
    coefficient = summed + bias_tile[:, None, :]
    rows_r = tile_rows[:, :rank, :].astype(jnp.float32)
    total = hidden.astype(jnp.float32)
    for r in range(rank):
        total = total + coefficient[:, :, r : r + 1] * rows_r[:, r : r + 1, :]
    return total.astype(jnp.bfloat16).reshape(rows_here, width)


def solution(mesh):
    devices = mesh.devices.reshape(mesh.shape["seq"] // 8, 4, 2, mesh.shape["chan"])
    split_mesh = Mesh(devices, ("y", "zh", "core", "chan"))
    in_specs = (
        P(None, SEQ, "chan"),
        P(None, "chan"),
        P(None, "chan"),
        P(SEQ, None, "chan"),
        P(),
        P(),
        P(),
    )
    out_specs = P(SEQ, "chan")
    return jax.shard_map(
        on_device, mesh=split_mesh, in_specs=in_specs, out_specs=out_specs, check_vma=False
    )
```

```python
import jax
import jax.numpy as jnp
from jax import lax
from jax.sharding import Mesh, PartitionSpec as P

TILE_ROWS = 128
SEQS = 4


SEQ = ("y", "zh", "core")


def shifted(block, distance):
    size = lax.axis_size(SEQ)
    return lax.ppermute(block, SEQ, [(i, (i + distance) % size) for i in range(size)])


def a2a_sum(block, axis):
    size = lax.axis_size(axis)
    copies = jnp.broadcast_to(block[None], (size,) + block.shape)
    return jnp.sum(lax.all_to_all(copies, axis, 0, 0, tiled=False), axis=0)


def depth_conv(window, taps_filter):
    width = window.shape[-1]
    kernel = taps_filter[::-1][:, None, :]
    return lax.conv_general_dilated(
        window,
        kernel,
        (1,),
        "VALID",
        dimension_numbers=("NWC", "WIO", "NWC"),
        feature_group_count=width,
        preferred_element_type=jnp.float32,
    )


def on_device(streams, short_filter, long_filter, edit_table, edit_bias, seq_tiles, seq_tenant):
    rows_here = streams.shape[1]
    width = streams.shape[2]
    short_reach = short_filter.shape[0]
    long_reach = long_filter.shape[0]
    tile_count = rows_here // TILE_ROWS
    me = lax.axis_index(SEQ)
    seq_ends = jnp.cumsum(seq_tiles)
    tile_ids = me * tile_count + jnp.arange(tile_count, dtype=jnp.int32)
    seq_of = jnp.sum((seq_ends[None, :] <= tile_ids[:, None]).astype(jnp.int32), axis=1)
    starts = (tile_ids == 0) | jnp.any(seq_ends[None, :] == tile_ids[:, None], axis=1)

    held = edit_table.shape[0]
    owner_slot = seq_tenant - me * held
    owned = (owner_slot >= 0) & (owner_slot < held)
    local_rows = jnp.take(edit_table, jnp.clip(owner_slot, 0, held - 1), axis=0)
    local_rows = jnp.where(owned[:, None, None], local_rows, jnp.zeros_like(local_rows))
    partial_rows = a2a_sum(local_rows, "zh")

    first_gate = streams[0].astype(jnp.float32)
    second_gate = streams[3].astype(jnp.float32)
    second_key = streams[4].astype(jnp.float32)
    gated = (streams[1].astype(jnp.float32) * streams[2].astype(jnp.float32)).astype(jnp.bfloat16)
    g_tiles = gated.reshape(tile_count, TILE_ROWS, width)

    def short_window(tile, earlier):
        earlier = jnp.where(starts[tile], jnp.zeros_like(earlier), earlier)
        return jnp.concatenate([earlier, g_tiles[tile]], axis=0)

    def carried_of(tile, short_out):
        rows = slice(tile * TILE_ROWS, (tile + 1) * TILE_ROWS)
        mixed = (first_gate[rows] * short_out).astype(jnp.bfloat16)
        return (second_key[rows] * mixed.astype(jnp.float32)).astype(jnp.bfloat16)

    later = [
        short_window(tile, g_tiles[tile - 1, TILE_ROWS - (short_reach - 1) :])
        for tile in range(1, tile_count)
    ]
    later_out = depth_conv(jnp.stack(later), short_filter)
    carried_later = [carried_of(tile, later_out[tile - 1]) for tile in range(1, tile_count)]

    border = jnp.concatenate(
        [gated[rows_here - (short_reach - 1) :], carried_later[-1][TILE_ROWS - (long_reach - 1) :]],
        axis=0,
    )
    row_count = partial_rows.shape[0] * partial_rows.shape[1]
    sent = jnp.concatenate([border, partial_rows.reshape(row_count, width)], axis=0)
    sent = shifted(sent, 1)
    short_border = sent[: short_reach - 1]
    long_border = sent[short_reach - 1 : border.shape[0]]
    chosen = partial_rows + sent[border.shape[0] :].reshape(partial_rows.shape)
    zh_size = lax.axis_size("y")
    stride = lax.axis_size("zh") * lax.axis_size("core")
    peer = me + (jnp.arange(zh_size, dtype=jnp.int32) - lax.axis_index("y")) * stride
    peer_tiles = peer[:, None] * tile_count + jnp.arange(tile_count, dtype=jnp.int32)[None, :]
    peer_seq = jnp.sum((seq_ends[None, None, :] <= peer_tiles[:, :, None]).astype(jnp.int32), axis=2)
    outgoing = jnp.zeros((zh_size, tile_count) + chosen.shape[1:], chosen.dtype)
    for s in range(SEQS):
        outgoing = jnp.where((peer_seq == s)[:, :, None, None], chosen[s], outgoing)
    tile_rows = jnp.sum(lax.all_to_all(outgoing, "y", 0, 0, tiled=False), axis=0)

    first_out = depth_conv(short_window(0, short_border)[None], short_filter)[0]
    carried = [carried_of(0, first_out)] + carried_later

    long_windows = []
    for tile in range(tile_count):
        earlier = long_border if tile == 0 else carried[tile - 1][TILE_ROWS - (long_reach - 1) :]
        earlier = jnp.where(starts[tile], jnp.zeros_like(earlier), earlier)
        long_windows.append(jnp.concatenate([earlier, carried[tile]], axis=0))
    long_out = depth_conv(jnp.stack(long_windows), long_filter)
    hidden = (second_gate.reshape(tile_count, TILE_ROWS, width) * long_out).astype(jnp.bfloat16)

    rows_per = edit_table.shape[1]
    rank = rows_per // 2
    projected = jnp.einsum(
        "tnc,trc->tnr", hidden, tile_rows, preferred_element_type=jnp.float32
    )
    partial = projected[..., rank:] - projected[..., :rank]
    summed = a2a_sum(partial, "chan")
    bias_tile = jnp.take(jnp.take(edit_bias, seq_tenant, axis=0), seq_of, axis=0)
    coefficient = summed + bias_tile[:, None, :]
    rows_r = tile_rows[:, :rank, :].astype(jnp.float32)
    total = hidden.astype(jnp.float32)
    for r in range(rank):
        total = total + coefficient[:, :, r : r + 1] * rows_r[:, r : r + 1, :]
    return total.astype(jnp.bfloat16).reshape(rows_here, width)


def solution(mesh):
    devices = mesh.devices.reshape(mesh.shape["seq"] // 8, 4, 2, mesh.shape["chan"])
    split_mesh = Mesh(devices, ("y", "zh", "core", "chan"))
    in_specs = (
        P(None, SEQ, "chan"),
        P(None, "chan"),
        P(None, "chan"),
        P(SEQ, None, "chan"),
        P(),
        P(),
        P(),
    )
    out_specs = P(SEQ, "chan")
    return jax.shard_map(
        on_device, mesh=split_mesh, in_specs=in_specs, out_specs=out_specs, check_vma=False
    )
```

```python
import jax
import jax.numpy as jnp
from jax import lax
from jax.sharding import Mesh, PartitionSpec as P

TILE_ROWS = 128
SEQS = 4


SEQ = ("y", "zh", "core")


def shifted(block, distance):
    size = lax.axis_size(SEQ)
    return lax.ppermute(block, SEQ, [(i, (i + distance) % size) for i in range(size)])


def a2a_sum(block, axis):
    size = lax.axis_size(axis)
    copies = jnp.broadcast_to(block[None], (size,) + block.shape)
    return jnp.sum(lax.all_to_all(copies, axis, 0, 0, tiled=False), axis=0)


def depth_conv(window, taps_filter):
    width = window.shape[-1]
    kernel = taps_filter[::-1][:, None, :]
    return lax.conv_general_dilated(
        window,
        kernel,
        (1,),
        "VALID",
        dimension_numbers=("NWC", "WIO", "NWC"),
        feature_group_count=width,
        preferred_element_type=jnp.float32,
    )


def on_device(streams, short_filter, long_filter, edit_table, edit_bias, seq_tiles, seq_tenant):
    rows_here = streams.shape[1]
    width = streams.shape[2]
    short_reach = short_filter.shape[0]
    long_reach = long_filter.shape[0]
    tile_count = rows_here // TILE_ROWS
    me = lax.axis_index(SEQ)
    seq_ends = jnp.cumsum(seq_tiles)
    tile_ids = me * tile_count + jnp.arange(tile_count, dtype=jnp.int32)
    seq_of = jnp.sum((seq_ends[None, :] <= tile_ids[:, None]).astype(jnp.int32), axis=1)
    starts = (tile_ids == 0) | jnp.any(seq_ends[None, :] == tile_ids[:, None], axis=1)

    held = edit_table.shape[0]
    owner_slot = seq_tenant - me * held
    picker = (owner_slot[:, None] == jnp.arange(held, dtype=jnp.int32)[None, :]).astype(edit_table.dtype)
    local_rows = jnp.einsum(
        "sh,hrc->src", picker, edit_table, preferred_element_type=jnp.float32
    ).astype(edit_table.dtype)
    partial_rows = a2a_sum(local_rows, "y")

    first_gate = streams[0].astype(jnp.float32)
    second_gate = streams[3].astype(jnp.float32)
    second_key = streams[4].astype(jnp.float32)
    gated = (streams[1].astype(jnp.float32) * streams[2].astype(jnp.float32)).astype(jnp.bfloat16)
    g_tiles = gated.reshape(tile_count, TILE_ROWS, width)

    def short_window(tile, earlier):
        earlier = jnp.where(starts[tile], jnp.zeros_like(earlier), earlier)
        return jnp.concatenate([earlier, g_tiles[tile]], axis=0)

    def carried_of(tile, short_out):
        rows = slice(tile * TILE_ROWS, (tile + 1) * TILE_ROWS)
        mixed = (first_gate[rows] * short_out).astype(jnp.bfloat16)
        return (second_key[rows] * mixed.astype(jnp.float32)).astype(jnp.bfloat16)

    later = [
        short_window(tile, g_tiles[tile - 1, TILE_ROWS - (short_reach - 1) :])
        for tile in range(1, tile_count)
    ]
    later_out = depth_conv(jnp.stack(later), short_filter)
    carried_later = [carried_of(tile, later_out[tile - 1]) for tile in range(1, tile_count)]

    border = jnp.concatenate(
        [gated[rows_here - (short_reach - 1) :], carried_later[-1][TILE_ROWS - (long_reach - 1) :]],
        axis=0,
    )
    row_count = partial_rows.shape[0] * partial_rows.shape[1]
    sent = jnp.concatenate([border, partial_rows.reshape(row_count, width)], axis=0)
    sent = shifted(sent, 1)
    short_border = sent[: short_reach - 1]
    long_border = sent[short_reach - 1 : border.shape[0]]
    chosen = partial_rows + sent[border.shape[0] :].reshape(partial_rows.shape)
    zh_size = lax.axis_size("zh")
    peer = me + (jnp.arange(zh_size, dtype=jnp.int32) - lax.axis_index("zh")) * lax.axis_size("core")
    peer_tiles = peer[:, None] * tile_count + jnp.arange(tile_count, dtype=jnp.int32)[None, :]
    peer_seq = jnp.sum((seq_ends[None, None, :] <= peer_tiles[:, :, None]).astype(jnp.int32), axis=2)
    outgoing = jnp.zeros((zh_size, tile_count) + chosen.shape[1:], chosen.dtype)
    for s in range(SEQS):
        outgoing = jnp.where((peer_seq == s)[:, :, None, None], chosen[s], outgoing)
    tile_rows = jnp.sum(lax.all_to_all(outgoing, "zh", 0, 0, tiled=False), axis=0)

    first_out = depth_conv(short_window(0, short_border)[None], short_filter)[0]
    carried = [carried_of(0, first_out)] + carried_later

    long_windows = []
    for tile in range(tile_count):
        earlier = long_border if tile == 0 else carried[tile - 1][TILE_ROWS - (long_reach - 1) :]
        earlier = jnp.where(starts[tile], jnp.zeros_like(earlier), earlier)
        long_windows.append(jnp.concatenate([earlier, carried[tile]], axis=0))
    long_out = depth_conv(jnp.stack(long_windows), long_filter)
    hidden = (second_gate.reshape(tile_count, TILE_ROWS, width) * long_out).astype(jnp.bfloat16)

    rows_per = edit_table.shape[1]
    rank = rows_per // 2
    projected = jnp.einsum(
        "tnc,trc->tnr", hidden, tile_rows, preferred_element_type=jnp.float32
    )
    partial = projected[..., rank:] - projected[..., :rank]
    summed = a2a_sum(partial, "chan")
    bias_tile = jnp.take(jnp.take(edit_bias, seq_tenant, axis=0), seq_of, axis=0)
    coefficient = summed + bias_tile[:, None, :]
    rows_r = tile_rows[:, :rank, :].astype(jnp.float32)
    total = hidden.astype(jnp.float32)
    for r in range(rank):
        total = total + coefficient[:, :, r : r + 1] * rows_r[:, r : r + 1, :]
    return total.astype(jnp.bfloat16).reshape(rows_here, width)


def solution(mesh):
    devices = mesh.devices.reshape(mesh.shape["seq"] // 8, 4, 2, mesh.shape["chan"])
    split_mesh = Mesh(devices, ("y", "zh", "core", "chan"))
    in_specs = (
        P(None, SEQ, "chan"),
        P(None, "chan"),
        P(None, "chan"),
        P(SEQ, None, "chan"),
        P(),
        P(),
        P(),
    )
    out_specs = P(SEQ, "chan")
    return jax.shard_map(
        on_device, mesh=split_mesh, in_specs=in_specs, out_specs=out_specs, check_vma=False
    )
```

```python
import jax
import jax.numpy as jnp
from jax import lax
from jax.sharding import Mesh, PartitionSpec as P

TILE_ROWS = 128
SEQS = 4


SEQ = ("y", "zh", "core")


def shifted(block, distance):
    size = lax.axis_size(SEQ)
    return lax.ppermute(block, SEQ, [(i, (i + distance) % size) for i in range(size)])


def a2a_sum(block, axis):
    size = lax.axis_size(axis)
    copies = jnp.broadcast_to(block[None], (size,) + block.shape)
    return jnp.sum(lax.all_to_all(copies, axis, 0, 0, tiled=False), axis=0)


def depth_conv(window, taps_filter):
    width = window.shape[-1]
    kernel = taps_filter[::-1][:, None, :]
    return lax.conv_general_dilated(
        window,
        kernel,
        (1,),
        "VALID",
        dimension_numbers=("NWC", "WIO", "NWC"),
        feature_group_count=width,
        preferred_element_type=jnp.float32,
    )


def on_device(streams, short_filter, long_filter, edit_table, edit_bias, seq_tiles, seq_tenant):
    rows_here = streams.shape[1]
    width = streams.shape[2]
    short_reach = short_filter.shape[0]
    long_reach = long_filter.shape[0]
    tile_count = rows_here // TILE_ROWS
    me = lax.axis_index(SEQ)
    seq_ends = jnp.cumsum(seq_tiles)
    tile_ids = me * tile_count + jnp.arange(tile_count, dtype=jnp.int32)
    seq_of = jnp.sum((seq_ends[None, :] <= tile_ids[:, None]).astype(jnp.int32), axis=1)
    starts = (tile_ids == 0) | jnp.any(seq_ends[None, :] == tile_ids[:, None], axis=1)

    held = edit_table.shape[0]
    owner_slot = seq_tenant - me * held
    picker = (owner_slot[:, None] == jnp.arange(held, dtype=jnp.int32)[None, :]).astype(edit_table.dtype)
    copies = jnp.broadcast_to(picker[None], (lax.axis_size("y"),) + picker.shape)
    local_copies = jnp.einsum(
        "nsh,hrc->nsrc", copies, edit_table, preferred_element_type=jnp.float32
    ).astype(edit_table.dtype)
    partial_rows = jnp.sum(lax.all_to_all(local_copies, "y", 0, 0, tiled=False), axis=0)

    first_gate = streams[0].astype(jnp.float32)
    second_gate = streams[3].astype(jnp.float32)
    second_key = streams[4].astype(jnp.float32)
    gated = (streams[1].astype(jnp.float32) * streams[2].astype(jnp.float32)).astype(jnp.bfloat16)
    g_tiles = gated.reshape(tile_count, TILE_ROWS, width)

    def short_window(tile, earlier):
        earlier = jnp.where(starts[tile], jnp.zeros_like(earlier), earlier)
        return jnp.concatenate([earlier, g_tiles[tile]], axis=0)

    def carried_of(tile, short_out):
        rows = slice(tile * TILE_ROWS, (tile + 1) * TILE_ROWS)
        mixed = (first_gate[rows] * short_out).astype(jnp.bfloat16)
        return (second_key[rows] * mixed.astype(jnp.float32)).astype(jnp.bfloat16)

    later = [
        short_window(tile, g_tiles[tile - 1, TILE_ROWS - (short_reach - 1) :])
        for tile in range(1, tile_count)
    ]
    later_out = depth_conv(jnp.stack(later), short_filter)
    carried_later = [carried_of(tile, later_out[tile - 1]) for tile in range(1, tile_count)]

    border = jnp.concatenate(
        [gated[rows_here - (short_reach - 1) :], carried_later[-1][TILE_ROWS - (long_reach - 1) :]],
        axis=0,
    )
    row_count = partial_rows.shape[0] * partial_rows.shape[1]
    sent = jnp.concatenate([border, partial_rows.reshape(row_count, width)], axis=0)
    sent = shifted(sent, 1)
    short_border = sent[: short_reach - 1]
    long_border = sent[short_reach - 1 : border.shape[0]]
    chosen = partial_rows + sent[border.shape[0] :].reshape(partial_rows.shape)
    zh_size = lax.axis_size("zh")
    peer = me + (jnp.arange(zh_size, dtype=jnp.int32) - lax.axis_index("zh")) * lax.axis_size("core")
    peer_tiles = peer[:, None] * tile_count + jnp.arange(tile_count, dtype=jnp.int32)[None, :]
    peer_seq = jnp.sum((seq_ends[None, None, :] <= peer_tiles[:, :, None]).astype(jnp.int32), axis=2)
    outgoing = jnp.zeros((zh_size, tile_count) + chosen.shape[1:], chosen.dtype)
    for s in range(SEQS):
        outgoing = jnp.where((peer_seq == s)[:, :, None, None], chosen[s], outgoing)
    tile_rows = jnp.sum(lax.all_to_all(outgoing, "zh", 0, 0, tiled=False), axis=0)

    first_out = depth_conv(short_window(0, short_border)[None], short_filter)[0]
    carried = [carried_of(0, first_out)] + carried_later

    long_windows = []
    for tile in range(tile_count):
        earlier = long_border if tile == 0 else carried[tile - 1][TILE_ROWS - (long_reach - 1) :]
        earlier = jnp.where(starts[tile], jnp.zeros_like(earlier), earlier)
        long_windows.append(jnp.concatenate([earlier, carried[tile]], axis=0))
    long_out = depth_conv(jnp.stack(long_windows), long_filter)
    hidden = (second_gate.reshape(tile_count, TILE_ROWS, width) * long_out).astype(jnp.bfloat16)

    rows_per = edit_table.shape[1]
    rank = rows_per // 2
    projected = jnp.einsum(
        "tnc,trc->tnr", hidden, tile_rows, preferred_element_type=jnp.float32
    )
    partial = projected[..., rank:] - projected[..., :rank]
    summed = a2a_sum(partial, "chan")
    bias_tile = jnp.take(jnp.take(edit_bias, seq_tenant, axis=0), seq_of, axis=0)
    coefficient = summed + bias_tile[:, None, :]
    rows_r = tile_rows[:, :rank, :].astype(jnp.float32)
    total = hidden.astype(jnp.float32)
    for r in range(rank):
        total = total + coefficient[:, :, r : r + 1] * rows_r[:, r : r + 1, :]
    return total.astype(jnp.bfloat16).reshape(rows_here, width)


def solution(mesh):
    devices = mesh.devices.reshape(mesh.shape["seq"] // 8, 4, 2, mesh.shape["chan"])
    split_mesh = Mesh(devices, ("y", "zh", "core", "chan"))
    in_specs = (
        P(None, SEQ, "chan"),
        P(None, "chan"),
        P(None, "chan"),
        P(SEQ, None, "chan"),
        P(),
        P(),
        P(),
    )
    out_specs = P(SEQ, "chan")
    return jax.shard_map(
        on_device, mesh=split_mesh, in_specs=in_specs, out_specs=out_specs, check_vma=False
    )
```

```python
import jax
import jax.numpy as jnp
from jax import lax
from jax.sharding import Mesh, PartitionSpec as P

TILE_ROWS = 128
SEQS = 4


SEQ = ("y", "zh", "core")


def shifted(block, distance):
    size = lax.axis_size(SEQ)
    return lax.ppermute(block, SEQ, [(i, (i + distance) % size) for i in range(size)])


def a2a_sum(block, axis):
    size = lax.axis_size(axis)
    copies = jnp.broadcast_to(block[None], (size,) + block.shape)
    return jnp.sum(lax.all_to_all(copies, axis, 0, 0, tiled=False), axis=0)


def depth_conv(window, taps_filter):
    width = window.shape[-1]
    kernel = taps_filter[::-1][:, None, :]
    return lax.conv_general_dilated(
        window,
        kernel,
        (1,),
        "VALID",
        dimension_numbers=("NWC", "WIO", "NWC"),
        feature_group_count=width,
        preferred_element_type=jnp.float32,
    )


def on_device(streams, short_filter, long_filter, edit_table, edit_bias, seq_tiles, seq_tenant):
    rows_here = streams.shape[1]
    width = streams.shape[2]
    short_reach = short_filter.shape[0]
    long_reach = long_filter.shape[0]
    tile_count = rows_here // TILE_ROWS
    me = lax.axis_index(SEQ)
    seq_ends = jnp.cumsum(seq_tiles)
    tile_ids = me * tile_count + jnp.arange(tile_count, dtype=jnp.int32)
    seq_of = jnp.sum((seq_ends[None, :] <= tile_ids[:, None]).astype(jnp.int32), axis=1)
    starts = (tile_ids == 0) | jnp.any(seq_ends[None, :] == tile_ids[:, None], axis=1)

    held = edit_table.shape[0]
    owner_slot = seq_tenant - me * held
    picker = (owner_slot[:, None] == jnp.arange(held, dtype=jnp.int32)[None, :]).astype(edit_table.dtype)
    local_rows = jnp.einsum(
        "sh,hrc->src", picker, edit_table, preferred_element_type=jnp.float32
    ).astype(edit_table.dtype)
    partial_rows = a2a_sum(local_rows, "y")

    first_gate = streams[0].astype(jnp.float32)
    second_gate = streams[3].astype(jnp.float32)
    second_key = streams[4].astype(jnp.float32)
    gated = (streams[1].astype(jnp.float32) * streams[2].astype(jnp.float32)).astype(jnp.bfloat16)
    g_tiles = gated.reshape(tile_count, TILE_ROWS, width)

    def short_window(tile, earlier):
        earlier = jnp.where(starts[tile], jnp.zeros_like(earlier), earlier)
        return jnp.concatenate([earlier, g_tiles[tile]], axis=0)

    def carried_of(tile, short_out):
        rows = slice(tile * TILE_ROWS, (tile + 1) * TILE_ROWS)
        mixed = (first_gate[rows] * short_out).astype(jnp.bfloat16)
        return (second_key[rows] * mixed.astype(jnp.float32)).astype(jnp.bfloat16)

    later = [
        short_window(tile, g_tiles[tile - 1, TILE_ROWS - (short_reach - 1) :])
        for tile in range(1, tile_count)
    ]
    later_out = depth_conv(jnp.stack(later), short_filter)
    carried_later = [carried_of(tile, later_out[tile - 1]) for tile in range(1, tile_count)]

    border = jnp.concatenate(
        [gated[rows_here - (short_reach - 1) :], carried_later[-1][TILE_ROWS - (long_reach - 1) :]],
        axis=0,
    )
    row_count = partial_rows.shape[0] * partial_rows.shape[1]
    sent = jnp.concatenate([border, partial_rows.reshape(row_count, width)], axis=0)
    sent = shifted(sent, 1)
    short_border = sent[: short_reach - 1]
    long_border = sent[short_reach - 1 : border.shape[0]]
    chosen = partial_rows + sent[border.shape[0] :].reshape(partial_rows.shape)
    zh_size = lax.axis_size("zh")
    peer = me + (jnp.arange(zh_size, dtype=jnp.int32) - lax.axis_index("zh")) * lax.axis_size("core")
    peer_tiles = peer[:, None] * tile_count + jnp.arange(tile_count, dtype=jnp.int32)[None, :]
    peer_seq = jnp.sum((seq_ends[None, None, :] <= peer_tiles[:, :, None]).astype(jnp.int32), axis=2)
    outgoing = jnp.zeros((zh_size, tile_count) + chosen.shape[1:], chosen.dtype)
    for s in range(SEQS):
        outgoing = jnp.where((peer_seq == s)[:, :, None, None], chosen[s], outgoing)
    tile_rows = jnp.sum(lax.all_to_all(outgoing, "zh", 0, 0, tiled=False), axis=0)

    first_out = depth_conv(short_window(0, short_border)[None], short_filter)[0]
    carried = [carried_of(0, first_out)] + carried_later

    long_windows = []
    for tile in range(tile_count):
        earlier = long_border if tile == 0 else carried[tile - 1][TILE_ROWS - (long_reach - 1) :]
        earlier = jnp.where(starts[tile], jnp.zeros_like(earlier), earlier)
        long_windows.append(jnp.concatenate([earlier, carried[tile]], axis=0))
    long_out = depth_conv(jnp.stack(long_windows), long_filter)
    hidden = (second_gate.reshape(tile_count, TILE_ROWS, width) * long_out).astype(jnp.bfloat16)

    rows_per = edit_table.shape[1]
    rank = rows_per // 2
    projected = jnp.einsum(
        "tnc,trc->tnr", hidden, tile_rows, preferred_element_type=jnp.float32
    )
    partial = projected[..., rank:] - projected[..., :rank]
    chan_size = lax.axis_size("chan")
    copies = jnp.broadcast_to(partial.astype(jnp.bfloat16)[None], (chan_size,) + partial.shape)
    received = lax.all_to_all(copies, "chan", 0, 0, tiled=False)
    summed = jnp.sum(received.astype(jnp.float32), axis=0)
    bias_tile = jnp.take(jnp.take(edit_bias, seq_tenant, axis=0), seq_of, axis=0)
    coefficient = summed + bias_tile[:, None, :]
    rows_r = tile_rows[:, :rank, :].astype(jnp.float32)
    total = hidden.astype(jnp.float32)
    for r in range(rank):
        total = total + coefficient[:, :, r : r + 1] * rows_r[:, r : r + 1, :]
    return total.astype(jnp.bfloat16).reshape(rows_here, width)


def solution(mesh):
    devices = mesh.devices.reshape(mesh.shape["seq"] // 8, 4, 2, mesh.shape["chan"])
    split_mesh = Mesh(devices, ("y", "zh", "core", "chan"))
    in_specs = (
        P(None, SEQ, "chan"),
        P(None, "chan"),
        P(None, "chan"),
        P(SEQ, None, "chan"),
        P(),
        P(),
        P(),
    )
    out_specs = P(SEQ, "chan")
    return jax.shard_map(
        on_device, mesh=split_mesh, in_specs=in_specs, out_specs=out_specs, check_vma=False
    )
```

```python
import jax
import jax.numpy as jnp
from jax import lax
from jax.sharding import Mesh, PartitionSpec as P

TILE_ROWS = 128
SEQS = 4


SEQ = ("y", "zh", "core")


def shifted(block, distance):
    size = lax.axis_size(SEQ)
    return lax.ppermute(block, SEQ, [(i, (i + distance) % size) for i in range(size)])


def a2a_sum(block, axis):
    size = lax.axis_size(axis)
    copies = jnp.broadcast_to(block[None], (size,) + block.shape)
    return jnp.sum(lax.all_to_all(copies, axis, 0, 0, tiled=False), axis=0)


def depth_conv(window, taps_filter):
    width = window.shape[-1]
    kernel = taps_filter[::-1][:, None, :]
    return lax.conv_general_dilated(
        window,
        kernel,
        (1,),
        "VALID",
        dimension_numbers=("NWC", "WIO", "NWC"),
        feature_group_count=width,
        preferred_element_type=jnp.float32,
    )


def on_device(streams, short_filter, long_filter, edit_table, edit_bias, seq_tiles, seq_tenant):
    rows_here = streams.shape[1]
    width = streams.shape[2]
    short_reach = short_filter.shape[0]
    long_reach = long_filter.shape[0]
    tile_count = rows_here // TILE_ROWS
    me = lax.axis_index(SEQ)
    seq_ends = jnp.cumsum(seq_tiles)
    tile_ids = me * tile_count + jnp.arange(tile_count, dtype=jnp.int32)
    seq_of = jnp.sum((seq_ends[None, :] <= tile_ids[:, None]).astype(jnp.int32), axis=1)
    starts = (tile_ids == 0) | jnp.any(seq_ends[None, :] == tile_ids[:, None], axis=1)

    held = edit_table.shape[0]
    owner_slot = seq_tenant - me * held
    picker = (owner_slot[:, None] == jnp.arange(held, dtype=jnp.int32)[None, :]).astype(edit_table.dtype)
    local_rows = jnp.einsum(
        "sh,hrc->src", picker, edit_table, preferred_element_type=jnp.float32
    ).astype(edit_table.dtype)
    partial_rows = a2a_sum(local_rows, "y")

    first_gate = streams[0].astype(jnp.float32)
    second_gate = streams[3].astype(jnp.float32)
    second_key = streams[4].astype(jnp.float32)
    gated = (streams[1].astype(jnp.float32) * streams[2].astype(jnp.float32)).astype(jnp.bfloat16)
    g_tiles = gated.reshape(tile_count, TILE_ROWS, width)

    def short_window(tile, earlier):
        earlier = jnp.where(starts[tile], jnp.zeros_like(earlier), earlier)
        return jnp.concatenate([earlier, g_tiles[tile]], axis=0)

    def carried_of(tile, short_out):
        rows = slice(tile * TILE_ROWS, (tile + 1) * TILE_ROWS)
        mixed = (first_gate[rows] * short_out).astype(jnp.bfloat16)
        return (second_key[rows] * mixed.astype(jnp.float32)).astype(jnp.bfloat16)

    later = [
        short_window(tile, g_tiles[tile - 1, TILE_ROWS - (short_reach - 1) :])
        for tile in range(1, tile_count)
    ]
    later_out = depth_conv(jnp.stack(later), short_filter)
    carried_later = [carried_of(tile, later_out[tile - 1]) for tile in range(1, tile_count)]

    border = jnp.concatenate(
        [gated[rows_here - (short_reach - 1) :], carried_later[-1][TILE_ROWS - (long_reach - 1) :]],
        axis=0,
    )
    row_count = partial_rows.shape[0] * partial_rows.shape[1]
    sent = jnp.concatenate([border, partial_rows.reshape(row_count, width)], axis=0)
    sent = shifted(sent, 1)
    short_border = sent[: short_reach - 1]
    long_border = sent[short_reach - 1 : border.shape[0]]
    chosen = partial_rows + sent[border.shape[0] :].reshape(partial_rows.shape)
    zh_size = lax.axis_size("zh")
    peer = me + (jnp.arange(zh_size, dtype=jnp.int32) - lax.axis_index("zh")) * lax.axis_size("core")
    peer_tiles = peer[:, None] * tile_count + jnp.arange(tile_count, dtype=jnp.int32)[None, :]
    peer_seq = jnp.sum((seq_ends[None, None, :] <= peer_tiles[:, :, None]).astype(jnp.int32), axis=2)
    outgoing = jnp.zeros((zh_size, tile_count) + chosen.shape[1:], chosen.dtype)
    for s in range(SEQS):
        outgoing = jnp.where((peer_seq == s)[:, :, None, None], chosen[s], outgoing)
    tile_rows = jnp.sum(lax.all_to_all(outgoing, "zh", 0, 0, tiled=False), axis=0)

    first_out = depth_conv(short_window(0, short_border)[None], short_filter)[0]
    carried = [carried_of(0, first_out)] + carried_later

    long_windows = []
    for tile in range(tile_count):
        earlier = long_border if tile == 0 else carried[tile - 1][TILE_ROWS - (long_reach - 1) :]
        earlier = jnp.where(starts[tile], jnp.zeros_like(earlier), earlier)
        long_windows.append(jnp.concatenate([earlier, carried[tile]], axis=0))
    long_out = depth_conv(jnp.stack(long_windows), long_filter)
    hidden = (second_gate.reshape(tile_count, TILE_ROWS, width) * long_out).astype(jnp.bfloat16)

    rows_per = edit_table.shape[1]
    rank = rows_per // 2
    chan_size = lax.axis_size("chan")
    row_copies = jnp.broadcast_to(tile_rows[None], (chan_size,) + tile_rows.shape)
    projected = jnp.einsum(
        "tnc,ktrc->ktnr", hidden, row_copies, preferred_element_type=jnp.float32
    )
    partial = projected[..., rank:] - projected[..., :rank]
    summed = jnp.sum(lax.all_to_all(partial, "chan", 0, 0, tiled=False), axis=0)
    bias_tile = jnp.take(jnp.take(edit_bias, seq_tenant, axis=0), seq_of, axis=0)
    coefficient = summed + bias_tile[:, None, :]
    rows_r = tile_rows[:, :rank, :].astype(jnp.float32)
    total = hidden.astype(jnp.float32)
    for r in range(rank):
        total = total + coefficient[:, :, r : r + 1] * rows_r[:, r : r + 1, :]
    return total.astype(jnp.bfloat16).reshape(rows_here, width)


def solution(mesh):
    devices = mesh.devices.reshape(mesh.shape["seq"] // 8, 4, 2, mesh.shape["chan"])
    split_mesh = Mesh(devices, ("y", "zh", "core", "chan"))
    in_specs = (
        P(None, SEQ, "chan"),
        P(None, "chan"),
        P(None, "chan"),
        P(SEQ, None, "chan"),
        P(),
        P(),
        P(),
    )
    out_specs = P(SEQ, "chan")
    return jax.shard_map(
        on_device, mesh=split_mesh, in_specs=in_specs, out_specs=out_specs, check_vma=False
    )
```
